256 devices in a mesh: expert: 16 (over x, y), dp: 16 (over z, core).
Axes of the slice: x: 4, y: 4, z: 8, core: 2. Of those that a mesh axis runs over, the one named last changes fastest.
Arguments:
- tokens: bfloat16 [4096, 4096], P(('expert', 'dp')), may hold values from -6 to 6
- grad_out: bfloat16 [4096, 4096], P(('expert', 'dp')), may hold values from -6 to 6
- gate_values: bfloat16 [4096, 2], P(('expert', 'dp')), may hold values from 0.099609375 to 1
- routes: int32 [4096, 2], P(('expert', 'dp')), may hold values from 0 to 31, all different within a row; in each aligned block of 16 rows (0 to 15, 16 to 31, ...) at most 2 rows name the same one
- gate_weight: bfloat16 [32, 1536, 4096], P('expert', 'dp'), may hold values from -0.09375 to 0.09375
- up_weight: bfloat16 [32, 1536, 4096], P('expert', 'dp'), may hold values from -0.09375 to 0.09375
- down_weight: bfloat16 [32, 1536, 4096], P('expert', 'dp'), may hold values from -0.15625 to 0.15625
Outputs:
- grad_tokens: bfloat16 [4096, 4096], P(('expert', 'dp'))
- grad_gates: float32 [4096, 2], P(('expert', 'dp'))
- grad_gate_weight: bfloat16 [32, 1536, 4096], P('expert', 'dp')
- grad_up_weight: bfloat16 [32, 1536, 4096], P('expert', 'dp')
- grad_down_weight: bfloat16 [32, 1536, 4096], P('expert', 'dp')
The draws below stay inside these ranges and needn't reach their ends.
Inputs may be any that keep to these rules, and one draw needn't show every extreme that they name: `routes`: each row names 2 different experts. In each aligned block of 16 rows (the rows of one device) no expert is named by more than 2 rows, a bound that some block reaches.
All inputs are finite; a program needn't handle non-finite values.
Results may differ from the reference program's by a relative error of at most 0.019.
Values may be sent and summed in bfloat16 or wider, within the bound.
No kernel may reach another device: no remote copies, remote signals or barrier semaphores. Data moves between devices by JAX's collectives and lax.ppermute only.
A program may use at most 128 MiB of HBM per device.

```python
import math
import jax
import jax.numpy as jnp
import numpy as np
from jax import lax

D = 4096
H = 1536
KWIN = 2
TOK_DEV = 16
EXPERTS = 32
CAP = 2
SLICE = 96
TOKENS = 4096
N_EXPERT = 16
N_DP = 16


def block_scale(rng, shape, cuts, low, largest):
    gain, own = 1.0, jax.random.fold_in(rng, 6)
    for axis_at, blocks in cuts:
        draws = jnp.exp(jax.random.uniform(jax.random.fold_in(own, axis_at), (blocks,), jnp.float32, low / len(cuts), largest / len(cuts)))
        gain = gain * jnp.repeat(draws, shape[axis_at] // blocks).reshape([-1 if axis == axis_at else 1 for axis in range(len(shape))])
    return gain


def shared_out(stream_key, own, number, rows, amount, top, bound, lean):
    ranking = jax.random.permutation(stream_key, amount)
    heavy_load, ordinary = portions_of(amount, rows * top, bound, lean, True), portions_of(amount, rows * top, bound, lean, False)
    places = jnp.arange(amount)

    def named(sizes, offset_by):
        used = int((sizes > 0).sum())
        fixed = max(1, used // 4)
        shifted = fixed + (places - fixed + offset_by * (used - fixed)) % max(1, amount - fixed)
        return jnp.zeros((amount,), jnp.int32).at[ranking[jnp.where(places < fixed, places, shifted)]].set(jnp.asarray(sizes, jnp.int32))

    sizes = jnp.where(number % 4 == 0, named(heavy_load, number // 4), named(ordinary, number - number // 4 - 1))
    mixed = jax.random.permutation(jax.random.fold_in(own, 3), amount)
    giver, taker = mixed[0:amount // 2 * 2:2], mixed[1:amount // 2 * 2:2]
    margin = jnp.minimum(sizes[giver] - 1, bound - sizes[taker]) // 2
    margin = jnp.where((giver == ranking[0]) | (taker == ranking[0]) | (sizes[taker] == 0), 0, jnp.maximum(margin, 0))
    shifted = jax.random.randint(jax.random.fold_in(own, 4), (amount // 2,), 0, 1 << 20) % (margin + 1)
    sizes = sizes.at[giver].add(-shifted).at[taker].add(shifted)
    labels = jnp.searchsorted(jnp.cumsum(sizes), jnp.arange(rows * top), side="right").astype(jnp.int32)
    listing = labels.reshape(top, rows).T
    listing = listing[jax.random.permutation(jax.random.fold_in(own, 1), rows)]
    offset_by = jax.random.randint(jax.random.fold_in(own, 2), (rows, 1), 0, top)
    return jnp.take_along_axis(listing, (jnp.arange(top)[None, :] + offset_by) % top, axis=1)


def portions_of(number_of, total, most, lean, full):
    weights = [(1 << 20) // math.isqrt(standing ** lean) + 1 for standing in range(1, number_of + 1)]
    largest = most if full else min(most, max(-(-total // number_of), total * weights[0] // sum(weights)))
    least = 1 if total - largest >= number_of - 1 else 0
    holding, spare = [largest] + [least] * (number_of - 1), total - largest - least * (number_of - 1)
    while spare > 0:
        movable = [i for i in range(1, number_of) if holding[i] < largest] or [i for i in range(1, number_of) if holding[i] < most]
        pool, left = sum([weights[i] for i in movable]), spare
        for i in movable:
            extra = min(most - holding[i], max(1, left * weights[i] // pool), spare)
            holding[i] = holding[i] + extra
            spare = spare - extra
    return np.array(holding)


def bell_draw(own_key, dims, deviation, most, shards=(), kind=jnp.bfloat16):
    drawn = deviation * jax.random.normal(own_key, dims, jnp.float32)
    if shards:
        drawn = drawn * block_scale(own_key, dims, shards, -0.22, 0.18)
    return jnp.clip(drawn, -most, most).astype(kind)


def setup_inputs(seed: int = 0) -> dict:
    splits = jax.random.split(jax.random.key(seed), 8)
    tokens = bell_draw(splits[0], (TOKENS, D), 1.0, 6.0, ((0, 256),))
    grad_out = bell_draw(splits[1], (TOKENS, D), 1.0, 6.0, ((0, 256),))
    gate_values = jnp.clip(jnp.exp(math.log(1.0) - 2.306499 * jax.random.uniform(splits[2], (TOKENS, KWIN), jnp.float32) ** block_scale(splits[2], (TOKENS, KWIN), ((0, 256),), -0.2, 0.2)), 0.099609375, 1.0).astype(jnp.bfloat16)
    routes_keys = jax.random.split(jax.random.fold_in(splits[3], 1), TOKENS // TOK_DEV)
    routes_turns = jax.random.permutation(jax.random.fold_in(splits[3], 3), TOKENS // TOK_DEV)
    routes = jax.vmap(lambda own, number: shared_out(jax.random.fold_in(splits[3], 2), own, number, TOK_DEV, EXPERTS, KWIN, CAP, 2))(routes_keys, routes_turns).reshape((TOKENS, KWIN))
    gate_weight = bell_draw(splits[4], (EXPERTS, H, D), D ** -0.5, 0.09375, ((0, 16), (1, 16)))
    up_weight = bell_draw(splits[5], (EXPERTS, H, D), D ** -0.5, 0.09375, ((0, 16), (1, 16)))
    down_weight = bell_draw(splits[6], (EXPERTS, H, D), H ** -0.5, 0.15625, ((0, 16), (1, 16)))
    return {"tokens": tokens, "grad_out": grad_out, "gate_values": gate_values, "routes": routes, "gate_weight": gate_weight, "up_weight": up_weight, "down_weight": down_weight}


def expert_terms(tokens, grad_out, flat_routes, flat_gates, gate_rows, up_rows, down_rows, expert):
    slot_total = N_EXPERT * N_DP * CAP
    picked = flat_routes == expert
    position = jnp.nonzero(picked, size=slot_total, fill_value=0)[0].astype(jnp.int32)
    live = (jnp.arange(slot_total) < jnp.sum(picked)).astype(jnp.float32)
    token_index = (position // KWIN).astype(jnp.int32)
    inputs = tokens[token_index]
    upstream = grad_out[token_index]
    weighting = (flat_gates[position] * live)[:, None]
    gate_pre = jnp.dot(inputs, gate_rows.T, preferred_element_type=jnp.float32)
    up_pre = jnp.dot(inputs, up_rows.T, preferred_element_type=jnp.float32)
    back_hidden = jnp.dot(upstream, down_rows.T, preferred_element_type=jnp.float32)
    sigmoid_gate = jax.nn.sigmoid(gate_pre)
    activated = gate_pre * sigmoid_gate
    hidden = activated * up_pre
    gate_grad = jnp.sum(back_hidden * hidden, axis=1)
    scaled = weighting * back_hidden
    grad_gate_pre = (scaled * up_pre * sigmoid_gate * (1.0 + gate_pre * (1.0 - sigmoid_gate))).astype(jnp.bfloat16)
    grad_up_pre = (scaled * activated).astype(jnp.bfloat16)
    weighted_hidden = (weighting * hidden).astype(jnp.bfloat16)
    split_gate = grad_gate_pre.astype(jnp.float32).reshape(slot_total, N_DP, SLICE)
    split_up = grad_up_pre.astype(jnp.float32).reshape(slot_total, N_DP, SLICE)
    gate_blocks = gate_rows.astype(jnp.float32).reshape(N_DP, SLICE, D)
    up_blocks = up_rows.astype(jnp.float32).reshape(N_DP, SLICE, D)
    pieces = jnp.einsum("rsh,shd->rsd", split_gate, gate_blocks, precision=lax.Precision.HIGHEST)
    pieces = pieces + jnp.einsum("rsh,shd->rsd", split_up, up_blocks, precision=lax.Precision.HIGHEST)
    pieces = lax.optimization_barrier(pieces.astype(jnp.bfloat16))
    row_grad = jnp.sum(pieces.astype(jnp.float32), axis=1).astype(jnp.bfloat16)
    grad_gate_rows = jnp.dot(grad_gate_pre.T, inputs, preferred_element_type=jnp.float32).astype(jnp.bfloat16)
    grad_up_rows = jnp.dot(grad_up_pre.T, inputs, preferred_element_type=jnp.float32).astype(jnp.bfloat16)
    grad_down_rows = jnp.dot(weighted_hidden.T, upstream, preferred_element_type=jnp.float32).astype(jnp.bfloat16)
    target = jnp.where(live > 0, position, TOKENS * KWIN).astype(jnp.int32)
    return row_grad, gate_grad, target, grad_gate_rows, grad_up_rows, grad_down_rows


def reference(tokens, grad_out, gate_values, routes, gate_weight, up_weight, down_weight):
    flat_routes = routes.reshape(-1)
    flat_gates = gate_values.reshape(-1).astype(jnp.float32)

    def per_expert(items):
        gate_rows, up_rows, down_rows, expert = items
        return expert_terms(tokens, grad_out, flat_routes, flat_gates, gate_rows, up_rows, down_rows, expert)

    experts_index = jnp.arange(EXPERTS, dtype=jnp.int32)
    row_grads, gate_grads, targets, grad_gate_weight, grad_up_weight, grad_down_weight = lax.map(
        per_expert, (gate_weight, up_weight, down_weight, experts_index))
    flat_targets = targets.reshape(-1)
    pair_grad = jnp.zeros((TOKENS * KWIN, D), jnp.float32).at[flat_targets].add(
        row_grads.reshape(-1, D).astype(jnp.float32), mode="drop")
    grad_tokens = jnp.sum(pair_grad.reshape(TOKENS, KWIN, D), axis=1).astype(jnp.bfloat16)
    grad_gates = jnp.zeros((TOKENS * KWIN,), jnp.float32).at[flat_targets].add(
        gate_grads.reshape(-1), mode="drop").reshape(TOKENS, KWIN)
    return grad_tokens, grad_gates, grad_gate_weight, grad_up_weight, grad_down_weight
```

```python
import jax
import jax.numpy as jnp
from jax import lax
from jax.sharding import Mesh
from jax.sharding import PartitionSpec as P

CORES = 2
PAD = 128


def per_device(tokens, grad_out, gate_values, routes, gate_weight, up_weight, down_weight):
    f32, bf16 = jnp.float32, jnp.bfloat16
    tok_rows, model_width = tokens.shape
    chosen = routes.shape[1]
    local_experts = gate_weight.shape[0]
    groups = lax.axis_size("expert")
    n_z = lax.axis_size("z")
    n_core = lax.axis_size("core")
    experts_all = local_experts * groups
    capacity = 2 * tok_rows * chosen // experts_all
    slot_count = experts_all * capacity
    block_rows = groups * capacity
    gathered_rows = n_core * n_z * block_rows
    width = 2 * model_width + PAD
    back_width = model_width + PAD

    flat_routes = routes.reshape(-1)
    onehot = (flat_routes[:, None] == jnp.arange(experts_all, dtype=jnp.int32)[None, :]).astype(
        jnp.int32
    )
    earlier = jnp.cumsum(onehot, axis=0) - onehot
    slot_rank = jnp.sum(earlier * onehot, axis=1)
    owner_col = flat_routes // local_experts
    local_id = flat_routes % local_experts
    slot_index = (local_id * groups + owner_col) * capacity + slot_rank
    placing = (jnp.arange(slot_count, dtype=jnp.int32)[:, None] == slot_index[None, :]).astype(f32)
    token_map = jnp.sum(placing.reshape(slot_count, tok_rows, chosen), axis=2).astype(bf16)
    slot_gates = jnp.dot(
        placing.astype(bf16), gate_values.reshape(-1), preferred_element_type=f32
    ).astype(bf16)
    x_slots = jnp.dot(token_map, tokens, preferred_element_type=f32).astype(bf16)
    dy_slots = jnp.dot(token_map, grad_out, preferred_element_type=f32).astype(bf16)
    gate_cols = jnp.concatenate(
        [slot_gates[:, None], jnp.zeros((slot_count, PAD - 1), bf16)], axis=1
    )
    payload = jnp.concatenate([x_slots, dy_slots, gate_cols], axis=1)
    payload = payload.reshape(local_experts, groups, capacity, width)

    backs, ggw, guw, gdw = [], [], [], []
    for l in range(local_experts):
        with jax.named_scope(f"expert_{l}"):
            blk = lax.all_to_all(payload[l], "expert", split_axis=0, concat_axis=0, tiled=True)
            blk = blk.reshape(block_rows, width)
            gz = lax.all_gather(blk, "z", axis=0)
            gzc = lax.all_gather(gz, "core", axis=0)
            rows = gzc.reshape(gathered_rows, width)
            inputs = rows[:, :model_width]
            upstream = rows[:, model_width : 2 * model_width]
            weighting = rows[:, 2 * model_width].astype(f32)[:, None]
            gw, uw, dw = gate_weight[l], up_weight[l], down_weight[l]
            gate_pre = jnp.einsum("rd,hd->rh", inputs, gw, preferred_element_type=f32)
            up_pre = jnp.einsum("rd,hd->rh", inputs, uw, preferred_element_type=f32)
            back_hidden = jnp.einsum("rd,hd->rh", upstream, dw, preferred_element_type=f32)
            sigmoid_gate = jax.nn.sigmoid(gate_pre)
            activated = gate_pre * sigmoid_gate
            hidden = activated * up_pre
            gate_part = jnp.sum(back_hidden * hidden, axis=1)
            scaled = weighting * back_hidden
            grad_gate_pre = (
                scaled * up_pre * sigmoid_gate * (1.0 + gate_pre * (1.0 - sigmoid_gate))
            ).astype(bf16)
            grad_up_pre = (scaled * activated).astype(bf16)
            weighted_hidden = (weighting * hidden).astype(bf16)
            input_part = jnp.einsum("rh,hd->rd", grad_gate_pre, gw, preferred_element_type=f32)
            input_part = input_part + jnp.einsum(
                "rh,hd->rd", grad_up_pre, uw, preferred_element_type=f32
            )
            hi = gate_part.astype(bf16)
            lo = (gate_part - hi.astype(f32)).astype(bf16)
            tail = jnp.concatenate(
                [hi[:, None], lo[:, None], jnp.zeros((gathered_rows, PAD - 2), bf16)], axis=1
            )
            back = jnp.concatenate([input_part.astype(bf16), tail], axis=1)
            back = back.reshape(n_core, n_z, block_rows, back_width)
            back = lax.psum_scatter(back, "core", scatter_dimension=0, tiled=True)
            back = lax.psum_scatter(back, "z", scatter_dimension=1, tiled=True)
            backs.append(back.reshape(groups, capacity, back_width))
            ggw.append(
                jnp.einsum("rh,rd->hd", grad_gate_pre, inputs, preferred_element_type=f32).astype(bf16)
            )
            guw.append(
                jnp.einsum("rh,rd->hd", grad_up_pre, inputs, preferred_element_type=f32).astype(bf16)
            )
            gdw.append(
                jnp.einsum("rh,rd->hd", weighted_hidden, upstream, preferred_element_type=f32).astype(
                    bf16
                )
            )

    back_all = jnp.stack(backs)
    returned = lax.all_to_all(back_all, "expert", split_axis=1, concat_axis=1, tiled=True)
    returned = returned.reshape(slot_count, back_width)
    grad_tokens = lax.dot_general(
        token_map,
        returned[:, :model_width],
        (((0,), (0,)), ((), ())),
        preferred_element_type=f32,
    ).astype(bf16)
    gate_back = returned[:, model_width].astype(f32) + returned[:, model_width + 1].astype(f32)
    grad_gates = jnp.dot(gate_back, placing, precision=lax.Precision.HIGHEST).reshape(
        tok_rows, chosen
    )
    return (grad_tokens, grad_gates, jnp.stack(ggw), jnp.stack(guw), jnp.stack(gdw))


def solution(mesh):
    n_expert, n_dp = mesh.devices.shape
    split = Mesh(mesh.devices.reshape(n_expert, n_dp // CORES, CORES), ("expert", "z", "core"))
    rows = P(("expert", "z", "core"), None)
    blocks = P("expert", ("z", "core"), None)
    return jax.shard_map(
        per_device,
        mesh=split,
        in_specs=(rows, rows, rows, rows, blocks, blocks, blocks),
        out_specs=(rows, rows, blocks, blocks, blocks),
        check_vma=False,
    )
```

```python
import jax
import jax.numpy as jnp
from jax import lax
from jax.sharding import PartitionSpec as P

PAD = 128


def per_device(tokens, grad_out, gate_values, routes, gate_weight, up_weight, down_weight):
    f32, bf16 = jnp.float32, jnp.bfloat16
    tok_rows, model_width = tokens.shape
    chosen = routes.shape[1]
    local_experts = gate_weight.shape[0]
    groups = lax.axis_size("expert")
    n_dp = lax.axis_size("dp")
    experts_all = local_experts * groups
    capacity = 2 * tok_rows * chosen // experts_all
    slot_count = experts_all * capacity
    block_rows = groups * capacity
    gathered_rows = n_dp * block_rows
    width = 2 * model_width + PAD
    back_width = model_width + PAD

    flat_routes = routes.reshape(-1)
    onehot = (flat_routes[:, None] == jnp.arange(experts_all, dtype=jnp.int32)[None, :]).astype(
        jnp.int32
    )
    earlier = jnp.cumsum(onehot, axis=0) - onehot
    slot_rank = jnp.sum(earlier * onehot, axis=1)
    owner_col = flat_routes // local_experts
    local_id = flat_routes % local_experts
    slot_index = (local_id * groups + owner_col) * capacity + slot_rank
    placing = (jnp.arange(slot_count, dtype=jnp.int32)[:, None] == slot_index[None, :]).astype(f32)
    token_map = jnp.sum(placing.reshape(slot_count, tok_rows, chosen), axis=2).astype(bf16)
    slot_gates = jnp.dot(
        placing.astype(bf16), gate_values.reshape(-1), preferred_element_type=f32
    ).astype(bf16)
    x_slots = jnp.dot(token_map, tokens, preferred_element_type=f32).astype(bf16)
    dy_slots = jnp.dot(token_map, grad_out, preferred_element_type=f32).astype(bf16)
    gate_cols = jnp.concatenate(
        [slot_gates[:, None], jnp.zeros((slot_count, PAD - 1), bf16)], axis=1
    )
    payload = jnp.concatenate([x_slots, dy_slots, gate_cols], axis=1)
    payload = payload.reshape(local_experts, groups, capacity, width)

    extra_rows = (
        jnp.arange(back_width, dtype=jnp.int32)[None, :]
        == model_width + jnp.arange(2, dtype=jnp.int32)[:, None]
    ).astype(bf16)
    backs, ggw, guw, gdw = [], [], [], []
    for l in range(local_experts):
        with jax.named_scope(f"expert_{l}"):
            blk = lax.all_to_all(payload[l], "expert", split_axis=0, concat_axis=0, tiled=True)
            blk = blk.reshape(block_rows, width)
            rows = lax.all_gather(blk, "dp", axis=0).reshape(gathered_rows, width)
            inputs = rows[:, :model_width]
            upstream = rows[:, model_width : 2 * model_width]
            weighting = rows[:, 2 * model_width].astype(f32)[:, None]
            gw, uw, dw = gate_weight[l], up_weight[l], down_weight[l]
            gate_pre = jnp.einsum("rd,hd->rh", inputs, gw, preferred_element_type=f32)
            up_pre = jnp.einsum("rd,hd->rh", inputs, uw, preferred_element_type=f32)
            back_hidden = jnp.einsum("rd,hd->rh", upstream, dw, preferred_element_type=f32)
            sigmoid_gate = jax.nn.sigmoid(gate_pre)
            activated = gate_pre * sigmoid_gate
            hidden = activated * up_pre
            gate_part = jnp.sum(back_hidden * hidden, axis=1)
            scaled = weighting * back_hidden
            grad_gate_pre = (
                scaled * up_pre * sigmoid_gate * (1.0 + gate_pre * (1.0 - sigmoid_gate))
            ).astype(bf16)
            grad_up_pre = (scaled * activated).astype(bf16)
            weighted_hidden = (weighting * hidden).astype(bf16)
            hi = gate_part.astype(bf16)
            lo = (gate_part - hi.astype(f32)).astype(bf16)
            lhs = jnp.concatenate([grad_gate_pre, grad_up_pre, hi[:, None], lo[:, None]], axis=1)
            stacked = jnp.pad(jnp.concatenate([gw, uw], axis=0), ((0, 0), (0, PAD)))
            rhs = jnp.concatenate([stacked, extra_rows], axis=0)
            back = jnp.dot(lhs, rhs, preferred_element_type=f32).astype(bf16)
            back = back.reshape(n_dp, block_rows, back_width)
            back = lax.psum_scatter(back, "dp", scatter_dimension=0, tiled=True)
            back = back.reshape(groups, capacity, back_width)
            backs.append(lax.all_to_all(back, "expert", split_axis=0, concat_axis=0, tiled=True))
            ggw.append(
                jnp.einsum("rh,rd->hd", grad_gate_pre, inputs, preferred_element_type=f32).astype(bf16)
            )
            guw.append(
                jnp.einsum("rh,rd->hd", grad_up_pre, inputs, preferred_element_type=f32).astype(bf16)
            )
            gdw.append(
                jnp.einsum("rh,rd->hd", weighted_hidden, upstream, preferred_element_type=f32).astype(
                    bf16
                )
            )

    returned = jnp.stack(backs).reshape(slot_count, back_width)
    grad_tokens = lax.dot_general(
        token_map,
        returned[:, :model_width],
        (((0,), (0,)), ((), ())),
        preferred_element_type=f32,
    ).astype(bf16)
    gate_back = returned[:, model_width].astype(f32) + returned[:, model_width + 1].astype(f32)
    grad_gates = jnp.dot(gate_back, placing, precision=lax.Precision.HIGHEST).reshape(
        tok_rows, chosen
    )
    return (grad_tokens, grad_gates, jnp.stack(ggw), jnp.stack(guw), jnp.stack(gdw))


def solution(mesh):
    rows = P(("expert", "dp"), None)
    blocks = P("expert", "dp", None)
    return jax.shard_map(
        per_device,
        mesh=mesh,
        in_specs=(rows, rows, rows, rows, blocks, blocks, blocks),
        out_specs=(rows, rows, blocks, blocks, blocks),
        check_vma=False,
    )
```

```python
import jax
import jax.numpy as jnp
from jax import lax
from jax.sharding import PartitionSpec as P

PAD = 128


def per_device(tokens, grad_out, gate_values, routes, gate_weight, up_weight, down_weight):
    f32, bf16 = jnp.float32, jnp.bfloat16
    tok_rows, model_width = tokens.shape
    chosen = routes.shape[1]
    local_experts = gate_weight.shape[0]
    groups = lax.axis_size("expert")
    n_dp = lax.axis_size("dp")
    experts_all = local_experts * groups
    capacity = 2 * tok_rows * chosen // experts_all
    slot_count = experts_all * capacity
    block_rows = groups * capacity
    gathered_rows = n_dp * block_rows
    width = 2 * model_width + PAD
    back_width = model_width + PAD

    flat_routes = routes.reshape(-1)
    onehot = (flat_routes[:, None] == jnp.arange(experts_all, dtype=jnp.int32)[None, :]).astype(
        jnp.int32
    )
    earlier = jnp.cumsum(onehot, axis=0) - onehot
    slot_rank = jnp.sum(earlier * onehot, axis=1)
    owner_col = flat_routes // local_experts
    local_id = flat_routes % local_experts
    slot_index = (local_id * groups + owner_col) * capacity + slot_rank
    placing = (jnp.arange(slot_count, dtype=jnp.int32)[:, None] == slot_index[None, :]).astype(f32)
    token_map = jnp.sum(placing.reshape(slot_count, tok_rows, chosen), axis=2).astype(bf16)
    slot_gates = jnp.dot(
        placing.astype(bf16), gate_values.reshape(-1), preferred_element_type=f32
    ).astype(bf16)
    x_slots = jnp.dot(token_map, tokens, preferred_element_type=f32).astype(bf16)
    dy_slots = jnp.dot(token_map, grad_out, preferred_element_type=f32).astype(bf16)
    gate_cols = jnp.concatenate(
        [slot_gates[:, None], jnp.zeros((slot_count, PAD - 1), bf16)], axis=1
    )
    payload = jnp.concatenate([x_slots, dy_slots, gate_cols], axis=1)
    payload = payload.reshape(local_experts, groups, capacity, width)

    extra_rows = (
        jnp.arange(back_width, dtype=jnp.int32)[None, :]
        == model_width + jnp.arange(2, dtype=jnp.int32)[:, None]
    ).astype(bf16)
    backs, ggw, guw, gdw = [], [], [], []
    for l in range(local_experts):
        with jax.named_scope(f"expert_{l}"):
            blk = lax.all_to_all(payload[l], "expert", split_axis=0, concat_axis=0, tiled=True)
            blk = blk.reshape(block_rows, width)
            rows = lax.all_gather(blk, "dp", axis=0).reshape(gathered_rows, width)
            inputs = rows[:, :model_width]
            upstream = rows[:, model_width : 2 * model_width]
            weighting = rows[:, 2 * model_width].astype(f32)[:, None]
            gw, uw, dw = gate_weight[l], up_weight[l], down_weight[l]
            gate_pre = jnp.einsum("rd,hd->rh", inputs, gw, preferred_element_type=f32)
            up_pre = jnp.einsum("rd,hd->rh", inputs, uw, preferred_element_type=f32)
            back_hidden = jnp.einsum("rd,hd->rh", upstream, dw, preferred_element_type=f32)
            sigmoid_gate = jax.nn.sigmoid(gate_pre)
            activated = gate_pre * sigmoid_gate
            hidden = activated * up_pre
            gate_part = jnp.sum(back_hidden * hidden, axis=1)
            scaled = weighting * back_hidden
            grad_gate_pre = (
                scaled * up_pre * sigmoid_gate * (1.0 + gate_pre * (1.0 - sigmoid_gate))
            ).astype(bf16)
            grad_up_pre = (scaled * activated).astype(bf16)
            weighted_hidden = (weighting * hidden).astype(bf16)
            hi = gate_part.astype(bf16)
            lo = (gate_part - hi.astype(f32)).astype(bf16)
            lhs = jnp.concatenate([grad_gate_pre, grad_up_pre, hi[:, None], lo[:, None]], axis=1)
            stacked = jnp.pad(jnp.concatenate([gw, uw], axis=0), ((0, 0), (0, PAD)))
            rhs = jnp.concatenate([stacked, extra_rows], axis=0)
            back = jnp.dot(lhs, rhs, preferred_element_type=f32).astype(bf16)
            backs.append(back.reshape(n_dp, block_rows, back_width))
            ggw.append(
                jnp.einsum("rh,rd->hd", grad_gate_pre, inputs, preferred_element_type=f32).astype(bf16)
            )
            guw.append(
                jnp.einsum("rh,rd->hd", grad_up_pre, inputs, preferred_element_type=f32).astype(bf16)
            )
            gdw.append(
                jnp.einsum("rh,rd->hd", weighted_hidden, upstream, preferred_element_type=f32).astype(
                    bf16
                )
            )

    back = lax.psum_scatter(jnp.concatenate(backs, axis=1), "dp", scatter_dimension=0, tiled=True)
    back = back.reshape(local_experts, groups, capacity, back_width)
    returned = lax.all_to_all(back, "expert", split_axis=1, concat_axis=1, tiled=True)
    returned = returned.reshape(slot_count, back_width)
    grad_tokens = lax.dot_general(
        token_map,
        returned[:, :model_width],
        (((0,), (0,)), ((), ())),
        preferred_element_type=f32,
    ).astype(bf16)
    gate_back = returned[:, model_width].astype(f32) + returned[:, model_width + 1].astype(f32)
    grad_gates = jnp.dot(gate_back, placing, precision=lax.Precision.HIGHEST).reshape(
        tok_rows, chosen
    )
    return (grad_tokens, grad_gates, jnp.stack(ggw), jnp.stack(guw), jnp.stack(gdw))


def solution(mesh):
    rows = P(("expert", "dp"), None)
    blocks = P("expert", "dp", None)
    return jax.shard_map(
        per_device,
        mesh=mesh,
        in_specs=(rows, rows, rows, rows, blocks, blocks, blocks),
        out_specs=(rows, rows, blocks, blocks, blocks),
        check_vma=False,
    )
```

```python
import jax
import jax.numpy as jnp
from jax import lax
from jax.sharding import PartitionSpec as P


PAD = 128


def per_device(tokens, grad_out, gate_values, routes, gate_weight, up_weight, down_weight):
    f32, bf16 = jnp.float32, jnp.bfloat16
    tok_rows, model_width = tokens.shape
    chosen = routes.shape[1]
    local_experts = gate_weight.shape[0]
    groups = lax.axis_size("expert")
    n_dp = lax.axis_size("dp")
    experts_all = local_experts * groups
    capacity = 2 * tok_rows * chosen // experts_all
    slot_count = experts_all * capacity
    block_rows = groups * capacity
    gathered_rows = n_dp * block_rows
    width = 2 * model_width + PAD
    back_width = model_width + PAD

    flat_routes = routes.reshape(-1)
    onehot = (flat_routes[:, None] == jnp.arange(experts_all, dtype=jnp.int32)[None, :]).astype(
        jnp.int32
    )
    earlier = jnp.cumsum(onehot, axis=0) - onehot
    slot_rank = jnp.sum(earlier * onehot, axis=1)
    owner_col = flat_routes // local_experts
    local_id = flat_routes % local_experts
    slot_index = (local_id * groups + owner_col) * capacity + slot_rank
    placing = (jnp.arange(slot_count, dtype=jnp.int32)[:, None] == slot_index[None, :]).astype(f32)
    token_map = jnp.sum(placing.reshape(slot_count, tok_rows, chosen), axis=2).astype(bf16)
    slot_gates = jnp.dot(
        placing.astype(bf16), gate_values.reshape(-1), preferred_element_type=f32
    ).astype(bf16)
    x_slots = jnp.dot(token_map, tokens, preferred_element_type=f32).astype(bf16)
    dy_slots = jnp.dot(token_map, grad_out, preferred_element_type=f32).astype(bf16)
    gate_cols = jnp.concatenate(
        [slot_gates[:, None], jnp.zeros((slot_count, PAD - 1), bf16)], axis=1
    )
    payload = jnp.concatenate([x_slots, dy_slots, gate_cols], axis=1)
    payload = payload.reshape(local_experts, groups, capacity, width)

    extra_rows = (
        jnp.arange(back_width, dtype=jnp.int32)[None, :]
        == model_width + jnp.arange(2, dtype=jnp.int32)[:, None]
    ).astype(bf16)
    backs, ggw, guw, gdw = [], [], [], []
    for l in range(local_experts):
        blk = lax.all_to_all(payload[l], "expert", split_axis=0, concat_axis=0, tiled=True)
        blk = blk.reshape(block_rows, width)
        rows = lax.all_gather(blk, "dp", axis=0).reshape(gathered_rows, width)
        inputs = rows[:, :model_width]
        upstream = rows[:, model_width : 2 * model_width]
        weighting = rows[:, 2 * model_width].astype(f32)[:, None]
        gw, uw, dw = gate_weight[l], up_weight[l], down_weight[l]
        gate_pre = jnp.einsum("rd,hd->rh", inputs, gw, preferred_element_type=f32)
        up_pre = jnp.einsum("rd,hd->rh", inputs, uw, preferred_element_type=f32)
        back_hidden = jnp.einsum("rd,hd->rh", upstream, dw, preferred_element_type=f32)
        sigmoid_gate = jax.nn.sigmoid(gate_pre)
        activated = gate_pre * sigmoid_gate
        hidden = activated * up_pre
        gate_part = jnp.sum(back_hidden * hidden, axis=1)
        scaled = weighting * back_hidden
        grad_gate_pre = (
            scaled * up_pre * sigmoid_gate * (1.0 + gate_pre * (1.0 - sigmoid_gate))
        ).astype(bf16)
        grad_up_pre = (scaled * activated).astype(bf16)
        weighted_hidden = (weighting * hidden).astype(bf16)
        hi = gate_part.astype(bf16)
        lo = (gate_part - hi.astype(f32)).astype(bf16)
        lhs = jnp.concatenate(
            [grad_gate_pre, grad_up_pre, hi[:, None], lo[:, None]], axis=1
        )
        stacked = jnp.pad(jnp.concatenate([gw, uw], axis=0), ((0, 0), (0, PAD)))
        rhs = jnp.concatenate([stacked, extra_rows], axis=0)
        back = jnp.dot(lhs, rhs, preferred_element_type=f32).astype(bf16)
        backs.append(back.reshape(n_dp, block_rows, back_width))
        ggw.append(
            jnp.einsum("rh,rd->hd", grad_gate_pre, inputs, preferred_element_type=f32).astype(bf16)
        )
        guw.append(
            jnp.einsum("rh,rd->hd", grad_up_pre, inputs, preferred_element_type=f32).astype(bf16)
        )
        gdw.append(
            jnp.einsum("rh,rd->hd", weighted_hidden, upstream, preferred_element_type=f32).astype(
                bf16
            )
        )

    back = lax.psum_scatter(jnp.concatenate(backs, axis=1), "dp", scatter_dimension=0, tiled=True)
    back = back.reshape(local_experts, groups, capacity, back_width)
    returned = lax.all_to_all(back, "expert", split_axis=1, concat_axis=1, tiled=True)
    returned = returned.reshape(slot_count, back_width)
    grad_tokens = lax.dot_general(
        token_map,
        returned[:, :model_width],
        (((0,), (0,)), ((), ())),
        preferred_element_type=f32,
    ).astype(bf16)
    gate_back = returned[:, model_width].astype(f32) + returned[:, model_width + 1].astype(f32)
    grad_gates = jnp.dot(gate_back, placing, precision=lax.Precision.HIGHEST).reshape(
        tok_rows, chosen
    )
    return (grad_tokens, grad_gates, jnp.stack(ggw), jnp.stack(guw), jnp.stack(gdw))


def solution(mesh):
    rows = P(("expert", "dp"), None)
    blocks = P("expert", "dp", None)
    return jax.shard_map(
        per_device,
        mesh=mesh,
        in_specs=(rows, rows, rows, rows, blocks, blocks, blocks),
        out_specs=(rows, rows, blocks, blocks, blocks),
        check_vma=False,
    )
```

```python
import jax
import jax.numpy as jnp
from jax import lax
from jax.sharding import PartitionSpec as P


PAD = 128


def per_device(tokens, grad_out, gate_values, routes, gate_weight, up_weight, down_weight):
    f32, bf16 = jnp.float32, jnp.bfloat16
    tok_rows, model_width = tokens.shape
    chosen = routes.shape[1]
    local_experts = gate_weight.shape[0]
    groups = lax.axis_size("expert")
    n_dp = lax.axis_size("dp")
    experts_all = local_experts * groups
    capacity = 2 * tok_rows * chosen // experts_all
    slot_count = experts_all * capacity
    block_rows = groups * capacity
    gathered_rows = n_dp * block_rows
    width = 2 * model_width + PAD
    back_width = model_width + PAD

    flat_routes = routes.reshape(-1)
    onehot = (flat_routes[:, None] == jnp.arange(experts_all, dtype=jnp.int32)[None, :]).astype(
        jnp.int32
    )
    earlier = jnp.cumsum(onehot, axis=0) - onehot
    slot_rank = jnp.sum(earlier * onehot, axis=1)
    owner_col = flat_routes // local_experts
    local_id = flat_routes % local_experts
    slot_index = (local_id * groups + owner_col) * capacity + slot_rank
    placing = (jnp.arange(slot_count, dtype=jnp.int32)[:, None] == slot_index[None, :]).astype(f32)
    token_map = jnp.sum(placing.reshape(slot_count, tok_rows, chosen), axis=2).astype(bf16)
    slot_gates = jnp.dot(
        placing.astype(bf16), gate_values.reshape(-1), preferred_element_type=f32
    ).astype(bf16)
    x_slots = jnp.dot(token_map, tokens, preferred_element_type=f32).astype(bf16)
    dy_slots = jnp.dot(token_map, grad_out, preferred_element_type=f32).astype(bf16)
    gate_cols = jnp.concatenate(
        [slot_gates[:, None], jnp.zeros((slot_count, PAD - 1), bf16)], axis=1
    )
    payload = jnp.concatenate([x_slots, dy_slots, gate_cols], axis=1)
    payload = payload.reshape(local_experts, groups, capacity, width)

    extra_rows = (
        jnp.arange(back_width, dtype=jnp.int32)[None, :]
        == model_width + jnp.arange(2, dtype=jnp.int32)[:, None]
    ).astype(bf16)
    ggw, guw, gdw = [], [], []
    for l in range(local_experts):
        blk = lax.all_to_all(payload[l], "expert", split_axis=0, concat_axis=0, tiled=True)
        blk = blk.reshape(block_rows, width)
        rows = lax.all_gather(blk, "dp", axis=0).reshape(gathered_rows, width)
        inputs = rows[:, :model_width]
        upstream = rows[:, model_width : 2 * model_width]
        weighting = rows[:, 2 * model_width].astype(f32)[:, None]
        gw, uw, dw = gate_weight[l], up_weight[l], down_weight[l]
        gate_pre = jnp.einsum("rd,hd->rh", inputs, gw, preferred_element_type=f32)
        up_pre = jnp.einsum("rd,hd->rh", inputs, uw, preferred_element_type=f32)
        back_hidden = jnp.einsum("rd,hd->rh", upstream, dw, preferred_element_type=f32)
        sigmoid_gate = jax.nn.sigmoid(gate_pre)
        activated = gate_pre * sigmoid_gate
        hidden = activated * up_pre
        gate_part = jnp.sum(back_hidden * hidden, axis=1)
        scaled = weighting * back_hidden
        grad_gate_pre = (
            scaled * up_pre * sigmoid_gate * (1.0 + gate_pre * (1.0 - sigmoid_gate))
        ).astype(bf16)
        grad_up_pre = (scaled * activated).astype(bf16)
        weighted_hidden = (weighting * hidden).astype(bf16)
        hi = gate_part.astype(bf16)
        lo = (gate_part - hi.astype(f32)).astype(bf16)
        lhs = jnp.concatenate(
            [grad_gate_pre, grad_up_pre, hi[:, None], lo[:, None]], axis=1
        )
        stacked = jnp.pad(jnp.concatenate([gw, uw], axis=0), ((0, 0), (0, PAD)))
        rhs = jnp.concatenate([stacked, extra_rows], axis=0)
        back = jnp.dot(lhs, rhs, preferred_element_type=f32).astype(bf16)
        back = back.reshape(n_dp, block_rows, back_width)
        if l == 0:
            merged = lax.optimization_barrier(jnp.pad(back, ((0, 0), (0, (local_experts - 1) * block_rows), (0, 0))))
        else:
            merged = lax.dynamic_update_slice_in_dim(merged, back, l * block_rows, axis=1)
        ggw.append(
            jnp.einsum("rh,rd->hd", grad_gate_pre, inputs, preferred_element_type=f32).astype(bf16)
        )
        guw.append(
            jnp.einsum("rh,rd->hd", grad_up_pre, inputs, preferred_element_type=f32).astype(bf16)
        )
        gdw.append(
            jnp.einsum("rh,rd->hd", weighted_hidden, upstream, preferred_element_type=f32).astype(
                bf16
            )
        )

    back = lax.psum_scatter(merged, "dp", scatter_dimension=0, tiled=True)
    back = back.reshape(local_experts, groups, capacity, back_width)
    returned = lax.all_to_all(back, "expert", split_axis=1, concat_axis=1, tiled=True)
    returned = returned.reshape(slot_count, back_width)
    grad_tokens = lax.dot_general(
        token_map,
        returned[:, :model_width],
        (((0,), (0,)), ((), ())),
        preferred_element_type=f32,
    ).astype(bf16)
    gate_back = returned[:, model_width].astype(f32) + returned[:, model_width + 1].astype(f32)
    grad_gates = jnp.dot(gate_back, placing, precision=lax.Precision.HIGHEST).reshape(
        tok_rows, chosen
    )
    return (grad_tokens, grad_gates, jnp.stack(ggw), jnp.stack(guw), jnp.stack(gdw))


def solution(mesh):
    rows = P(("expert", "dp"), None)
    blocks = P("expert", "dp", None)
    return jax.shard_map(
        per_device,
        mesh=mesh,
        in_specs=(rows, rows, rows, rows, blocks, blocks, blocks),
        out_specs=(rows, rows, blocks, blocks, blocks),
        check_vma=False,
    )
```

```python
import jax
import jax.numpy as jnp
from jax import lax
from jax.sharding import PartitionSpec as P


PAD = 128


def shifted(n, k):
    return [(i, (i + k) % n) for i in range(n)]


def per_device(tokens, grad_out, gate_values, routes, gate_weight, up_weight, down_weight):
    f32, bf16 = jnp.float32, jnp.bfloat16
    tok_rows, model_width = tokens.shape
    chosen = routes.shape[1]
    local_experts = gate_weight.shape[0]
    groups = lax.axis_size("expert")
    n_dp = lax.axis_size("dp")
    experts_all = local_experts * groups
    capacity = 2 * tok_rows * chosen // experts_all
    slot_count = experts_all * capacity
    block_rows = groups * capacity
    gathered_rows = n_dp * block_rows
    width = 2 * model_width + PAD
    back_width = model_width + PAD

    flat_routes = routes.reshape(-1)
    onehot = (flat_routes[:, None] == jnp.arange(experts_all, dtype=jnp.int32)[None, :]).astype(
        jnp.int32
    )
    earlier = jnp.cumsum(onehot, axis=0) - onehot
    slot_rank = jnp.sum(earlier * onehot, axis=1)
    owner_col = (flat_routes // local_experts - lax.axis_index("expert")) % groups
    local_id = flat_routes % local_experts
    slot_index = (local_id * groups + owner_col) * capacity + slot_rank
    placing = (jnp.arange(slot_count, dtype=jnp.int32)[:, None] == slot_index[None, :]).astype(f32)
    token_map = jnp.sum(placing.reshape(slot_count, tok_rows, chosen), axis=2).astype(bf16)
    slot_gates = jnp.dot(
        placing.astype(bf16), gate_values.reshape(-1), preferred_element_type=f32
    ).astype(bf16)
    x_slots = jnp.dot(token_map, tokens, preferred_element_type=f32).astype(bf16)
    dy_slots = jnp.dot(token_map, grad_out, preferred_element_type=f32).astype(bf16)
    gate_cols = jnp.concatenate(
        [slot_gates[:, None], jnp.zeros((slot_count, PAD - 1), bf16)], axis=1
    )
    payload = jnp.concatenate([x_slots, dy_slots, gate_cols], axis=1)
    payload = payload.reshape(local_experts, groups, capacity, width)
    arrived = [payload[:, 0]] + [
        lax.ppermute(payload[:, k], "expert", shifted(groups, k)) for k in range(1, groups)
    ]

    extra_rows = (
        jnp.arange(back_width, dtype=jnp.int32)[None, :]
        == model_width + jnp.arange(2, dtype=jnp.int32)[:, None]
    ).astype(bf16)
    ggw, guw, gdw = [], [], []
    for l in range(local_experts):
        blk = jnp.stack([part[l] for part in arrived]).reshape(block_rows, width)
        rows = lax.all_gather(blk, "dp", axis=0).reshape(gathered_rows, width)
        inputs = rows[:, :model_width]
        upstream = rows[:, model_width : 2 * model_width]
        weighting = rows[:, 2 * model_width].astype(f32)[:, None]
        gw, uw, dw = gate_weight[l], up_weight[l], down_weight[l]
        gate_pre = jnp.einsum("rd,hd->rh", inputs, gw, preferred_element_type=f32)
        up_pre = jnp.einsum("rd,hd->rh", inputs, uw, preferred_element_type=f32)
        back_hidden = jnp.einsum("rd,hd->rh", upstream, dw, preferred_element_type=f32)
        sigmoid_gate = jax.nn.sigmoid(gate_pre)
        activated = gate_pre * sigmoid_gate
        hidden = activated * up_pre
        gate_part = jnp.sum(back_hidden * hidden, axis=1)
        scaled = weighting * back_hidden
        grad_gate_pre = (
            scaled * up_pre * sigmoid_gate * (1.0 + gate_pre * (1.0 - sigmoid_gate))
        ).astype(bf16)
        grad_up_pre = (scaled * activated).astype(bf16)
        weighted_hidden = (weighting * hidden).astype(bf16)
        hi = gate_part.astype(bf16)
        lo = (gate_part - hi.astype(f32)).astype(bf16)
        lhs = jnp.concatenate(
            [grad_gate_pre, grad_up_pre, hi[:, None], lo[:, None]], axis=1
        )
        stacked = jnp.pad(jnp.concatenate([gw, uw], axis=0), ((0, 0), (0, PAD)))
        rhs = jnp.concatenate([stacked, extra_rows], axis=0)
        back = jnp.dot(lhs, rhs, preferred_element_type=f32).astype(bf16)
        back = back.reshape(n_dp, block_rows, back_width)
        if l == 0:
            merged = lax.optimization_barrier(jnp.pad(back, ((0, 0), (0, (local_experts - 1) * block_rows), (0, 0))))
        else:
            merged = lax.dynamic_update_slice_in_dim(merged, back, l * block_rows, axis=1)
        ggw.append(
            jnp.einsum("rh,rd->hd", grad_gate_pre, inputs, preferred_element_type=f32).astype(bf16)
        )
        guw.append(
            jnp.einsum("rh,rd->hd", grad_up_pre, inputs, preferred_element_type=f32).astype(bf16)
        )
        gdw.append(
            jnp.einsum("rh,rd->hd", weighted_hidden, upstream, preferred_element_type=f32).astype(
                bf16
            )
        )

    back = lax.psum_scatter(merged, "dp", scatter_dimension=0, tiled=True)
    back = back.reshape(local_experts, groups, capacity, back_width)
    sent_back = [back[:, 0]] + [
        lax.ppermute(back[:, k], "expert", shifted(groups, -k)) for k in range(1, groups)
    ]
    returned = jnp.stack(sent_back, axis=1).reshape(slot_count, back_width)
    grad_tokens = lax.dot_general(
        token_map,
        returned[:, :model_width],
        (((0,), (0,)), ((), ())),
        preferred_element_type=f32,
    ).astype(bf16)
    gate_back = returned[:, model_width].astype(f32) + returned[:, model_width + 1].astype(f32)
    grad_gates = jnp.dot(gate_back, placing, precision=lax.Precision.HIGHEST).reshape(
        tok_rows, chosen
    )
    return (grad_tokens, grad_gates, jnp.stack(ggw), jnp.stack(guw), jnp.stack(gdw))


def solution(mesh):
    rows = P(("expert", "dp"), None)
    blocks = P("expert", "dp", None)
    return jax.shard_map(
        per_device,
        mesh=mesh,
        in_specs=(rows, rows, rows, rows, blocks, blocks, blocks),
        out_specs=(rows, rows, blocks, blocks, blocks),
        check_vma=False,
    )
```
